32 devices in a mesh: dp: 8 (over z, y), tensor: 4 (over x, core).
Axes of the slice: x: 2, y: 2, z: 4, core: 2. Of those that a mesh axis runs over, the one named last changes fastest.
Arguments:
- hidden_in: bfloat16 [32768, 768], P(('dp', 'tensor')), may hold values from -6 to 6
- qkv_weight: bfloat16 [3, 768, 768], P(None, 'tensor'), may hold values from -0.21875 to 0.21875
- qv_bias: bfloat16 [2, 768], P(None, 'tensor'), may hold values from -3 to 3
- out_weight: bfloat16 [768, 768], P('tensor'), may hold values from -1.25 to 1.25
- out_bias: bfloat16 [768], replicated, may hold values from -3 to 3
- norm1_gain: bfloat16 [768], replicated, may hold values from 0.25 to 1.75
- norm1_shift: bfloat16 [768], replicated, may hold values from -3 to 3
- up_weight: bfloat16 [3072, 768], P('tensor'), may hold values from -0.21875 to 0.21875
- up_bias: bfloat16 [3072], P('tensor'), may hold values from -3 to 3
- down_weight: bfloat16 [3072, 768], P('tensor'), may hold values from -0.109375 to 0.109375
- down_bias: bfloat16 [768], replicated, may hold values from -3 to 3
- norm2_gain: bfloat16 [768], replicated, may hold values from 0.25 to 1.75
- norm2_shift: bfloat16 [768], replicated, may hold values from -3 to 3
- out_grad: bfloat16 [32768, 768], P(('dp', 'tensor')), may hold values from -12 to 12
- seq_lengths: int32 [256], P('dp'), may hold values from 32 to 128, as said below
- key_mask: int32 [32768], P('dp'), may hold values 0 or 1
- split_pos: int32 [256], P('dp'), may hold values from 8 to 95, as said below
Outputs:
- layer_out: bfloat16 [32768, 768], P(('dp', 'tensor'))
- input_grad: bfloat16 [32768, 768], P(('dp', 'tensor'))
- grad_qkv_weight: float32 [3, 768, 768], P(None, 'tensor')
- grad_qv_bias: float32 [2, 768], P(None, 'tensor')
- grad_out_weight: float32 [768, 768], P('tensor')
- grad_out_bias: float32 [768], replicated
- grad_norm1_gain: float32 [768], replicated
- grad_norm1_shift: float32 [768], replicated
- grad_up_weight: float32 [3072, 768], P('tensor')
- grad_up_bias: float32 [3072], P('tensor')
- grad_down_weight: float32 [3072, 768], P('tensor')
- grad_down_bias: float32 [768], replicated
- grad_norm2_gain: float32 [768], replicated
- grad_norm2_shift: float32 [768], replicated
The draws below stay inside these ranges and needn't reach their ends.
Inputs may be any that keep to these rules, and one draw needn't show every extreme that they name: `seq_lengths`: every slot's length is at least a quarter of 128; the first slot of each index of dp is full. `split_pos`: a slot's split position is at least its length // 4 (a quarter, rounded down) and below three quarters of it.
All inputs are finite; a program needn't handle non-finite values. No bound on the sum of `key_mask` on one device may be relied on, other than what follows from the above.
Results may differ from the reference program's by a relative error of at most 0.019.
Values may be sent and summed in bfloat16 or wider, within the bound.
No kernel may reach another device: no remote copies, remote signals or barrier semaphores. Data moves between devices by JAX's collectives and lax.ppermute only.
A program may use at most 192 MiB of HBM per device.

```python
from functools import partial
import jax
import jax.numpy as jnp
from jax import lax

D = 768
HD = 64
FF = 3072
SLOT = 128
SEQ_DEV = 32
TOK_DEV = 4096
SEQS = 256
TOKENS = 32768
N_DP = 8


def draw_slots(key):
    base_key = jax.random.fold_in(key, 11)
    key_level, key_long, key_short, key_coin, key_split = jax.random.split(base_key, 5)
    groups = SEQS // SEQ_DEV
    group_level = jax.random.randint(key_level, (groups, 1), 1, 4)
    slot_coin = jax.random.randint(key_coin, (groups, SEQ_DEV), 0, 4)
    long_len = jax.random.randint(key_long, (groups, SEQ_DEV), SLOT // 2 + 1, SLOT + 1)
    short_len = jax.random.randint(key_short, (groups, SEQ_DEV), SLOT // 4, SLOT // 2 + 1)
    lengths = jnp.where(slot_coin < group_level, long_len, short_len)
    first_slot = jnp.arange(SEQ_DEV)[None, :] == 0
    lengths = jnp.where(first_slot, SLOT, lengths).reshape(SEQS).astype(jnp.int32)
    spread = jax.random.randint(key_split, (SEQS,), 0, 1 << 20)
    split_place = (lengths // 4 + spread % (lengths // 2)).astype(jnp.int32)
    return (lengths, split_place)


def draw_seq_lengths(key, part):
    lengths, split_place = draw_slots(key)
    return lengths


def draw_split_pos(key, part):
    lengths, split_place = draw_slots(key)
    return split_place


def draw_out_grad(key, part):
    key_primary = jax.random.fold_in(jax.random.fold_in(key, 3), 0)
    row_index = jnp.arange(TOKENS, dtype=jnp.float32)[:, None]
    row_rise = 1.0 + 2.0 * row_index / max(TOKENS - 1, 1)
    values = jax.random.normal(key_primary, (TOKENS, D), jnp.float32) * row_rise
    return jnp.clip(values, -12.0, 12.0).astype(jnp.bfloat16)


def set_ends(entries, key, smallest, high):
    spot = [jax.random.randint(jax.random.fold_in(key, axis), (), 0, length) for axis, length in enumerate(entries.shape)]
    main_axis = entries.shape.index(max(entries.shape))
    beside = spot[:main_axis] + [(spot[main_axis] + 1) % entries.shape[main_axis]] + spot[main_axis + 1:]
    return entries.at[tuple(spot)].set(smallest).at[tuple(beside)].set(high)


def level_of(key, extent, shards, least, top_value):
    def one(position, shards_of):
        steps = jax.random.uniform(jax.random.fold_in(jax.random.fold_in(key, 6), position), (shards_of,), jnp.float32, least / len(shards), top_value / len(shards))
        return jnp.repeat(jnp.exp(steps), extent[position] // shards_of).reshape((-1,) + (1,) * (len(extent) - position - 1))

    level = one(*shards[0])
    for cut in shards[1:]:
        level = level * one(*cut)
    return level


def scatter_about(own_key, shape, scale, bound, cuts=(), kind=jnp.bfloat16):
    result = scale * jax.random.normal(own_key, shape, jnp.float32)
    if cuts:
        result = result * level_of(own_key, shape, cuts, -0.22, 0.18)
    return jnp.clip(result, -bound, bound).astype(kind)


def setup_inputs(seed: int = 0) -> dict:
    splits = jax.random.split(jax.random.key(seed), 18)
    return {
        "hidden_in": scatter_about(splits[0], (TOKENS, D), 1.0, 6.0, ((0, 32),)),
        "qkv_weight": scatter_about(splits[1], (3, D, D), D ** -0.5, 0.21875, ((1, 4),)),
        "qv_bias": scatter_about(splits[2], (2, D), 0.5, 3.0, ((1, 4),)),
        "out_weight": scatter_about(splits[3], (D, D), (D // 32) ** -0.5, 1.25, ((0, 4),)),
        "out_bias": scatter_about(splits[4], (D,), 0.5, 3.0),
        "norm1_gain": jnp.clip(1.0 + 0.15 * jax.random.normal(splits[5], (D,), jnp.float32), 0.25, 1.75).astype(jnp.bfloat16),
        "norm1_shift": scatter_about(splits[6], (D,), 0.5, 3.0),
        "up_weight": scatter_about(splits[7], (FF, D), D ** -0.5, 0.21875, ((0, 4),)),
        "up_bias": scatter_about(splits[8], (FF,), 0.5, 3.0, ((0, 4),)),
        "down_weight": scatter_about(splits[9], (FF, D), FF ** -0.5, 0.109375, ((0, 4),)),
        "down_bias": scatter_about(splits[10], (D,), 0.5, 3.0),
        "norm2_gain": jnp.clip(1.0 + 0.15 * jax.random.normal(splits[11], (D,), jnp.float32), 0.25, 1.75).astype(jnp.bfloat16),
        "norm2_shift": scatter_about(splits[12], (D,), 0.5, 3.0),
        "out_grad": draw_out_grad(jax.random.fold_in(splits[17], 71), 0),
        "seq_lengths": draw_seq_lengths(jax.random.fold_in(splits[17], 71), 0),
        "key_mask": set_ends((jax.random.randint(splits[15], (TOKENS,), 0, 8) < 7).astype(jnp.int32), jax.random.fold_in(splits[15], 1), 0, 1),
        "split_pos": draw_split_pos(jax.random.fold_in(splits[17], 71), 0),
    }


HIGHEST = lax.Precision.HIGHEST
EPSILON = 1e-05
ROOT_HALF = 0.7071067811865476

@jax.custom_vjp
def low(v):
    return lax.optimization_barrier(v.astype(jnp.bfloat16)).astype(jnp.float32)

@jax.custom_vjp
def low_back(v):
    return v

def low_keep(v):
    return (low(v), None)

def low_pass(kept, grad):
    return (grad,)

def back_keep(v):
    return (v, None)

def back_low(kept, grad):
    return (low(grad),)
low.defvjp(low_keep, low_pass)
low_back.defvjp(back_keep, back_low)

def layer_norm(hidden, norm_gain, norm_offset):
    average = lax.optimization_barrier(jnp.mean(hidden, axis=1, keepdims=True))
    centred = hidden - average
    spread = lax.optimization_barrier(jnp.mean(centred * centred, axis=1, keepdims=True))
    return centred * lax.rsqrt(spread + EPSILON) * norm_gain + norm_offset

def attend(operands):
    queries, key_rows, value_rows, valid_keys = operands
    raw_scores = jnp.einsum('bqhe,bkhe->bhqk', queries, key_rows, precision=HIGHEST)
    scores = low_back(raw_scores * HD ** (-0.5))
    masked = jnp.where(valid_keys[:, None, None, :], scores, -1e+30)
    largest = lax.optimization_barrier(jnp.max(masked, axis=-1, keepdims=True))
    weights_raw = jnp.exp(masked - largest)
    probability = low(weights_raw / lax.optimization_barrier(jnp.sum(weights_raw, axis=-1, keepdims=True)))
    context = jnp.einsum('bhqk,bkhe->bqhe', probability, value_rows, precision=HIGHEST)
    return low_back(low(context))

def forward(params, rows_in, valid_blocks):
    qkv_weight, qv_bias, out_weight, out_bias, norm1_gain, norm1_shift, up_weight, up_bias, down_weight, down_bias, norm2_gain, norm2_shift = params
    group_rows = rows_in.shape[0]
    block_count, per_block, slot_len = valid_blocks.shape
    heads_all = qkv_weight.shape[1] // HD
    projected = jnp.einsum('rd,cld->crl', rows_in, qkv_weight, precision=HIGHEST)
    bias_rows = jnp.stack([qv_bias[0], jnp.zeros_like(qv_bias[0]), qv_bias[1]])
    projected = low_back(low(projected + bias_rows[:, None, :]))
    head_shape = (block_count, per_block, slot_len, heads_all, HD)
    context = lax.map(jax.checkpoint(attend), (projected[0].reshape(head_shape), projected[1].reshape(head_shape), projected[2].reshape(head_shape), valid_blocks))
    context_rows = context.reshape(group_rows, heads_all * HD)
    attn_out = low_back(jnp.dot(context_rows, out_weight, precision=HIGHEST))
    mid_rows = layer_norm(rows_in + attn_out + out_bias, norm1_gain, norm1_shift)
    before = low_back(jnp.dot(low(mid_rows), up_weight.T, precision=HIGHEST) + up_bias)
    activated = low(before * 0.5 * (1.0 + jax.scipy.special.erf(before * ROOT_HALF)))
    ffn_out = low_back(jnp.dot(activated, down_weight, precision=HIGHEST))
    return layer_norm(mid_rows + ffn_out + down_bias, norm2_gain, norm2_shift)

def reference(hidden_in, qkv_weight, qv_bias, out_weight, out_bias, norm1_gain, norm1_shift, up_weight, up_bias, down_weight, down_bias, norm2_gain, norm2_shift, out_grad, seq_lengths, key_mask, split_pos):
    weights = (qkv_weight.astype(jnp.float32), qv_bias.astype(jnp.float32), out_weight.astype(jnp.float32), out_bias.astype(jnp.float32), norm1_gain.astype(jnp.float32), norm1_shift.astype(jnp.float32), up_weight.astype(jnp.float32), up_bias.astype(jnp.float32), down_weight.astype(jnp.float32), down_bias.astype(jnp.float32), norm2_gain.astype(jnp.float32), norm2_shift.astype(jnp.float32))
    per_block = max(1, min(SEQ_DEV, 512 // SLOT))
    block_count = SEQ_DEV // per_block
    places = lax.broadcasted_iota(jnp.int32, (N_DP, SEQ_DEV, SLOT), 2)
    lengths = seq_lengths.reshape(N_DP, SEQ_DEV, 1)
    valid_all = (places < lengths) & ((key_mask.reshape(N_DP, SEQ_DEV, SLOT) == 1) | (places == 0))
    target = ((places >= split_pos.reshape(N_DP, SEQ_DEV, 1)) & (places < lengths)).astype(jnp.float32).reshape(N_DP, TOK_DEV, 1)
    rows_all = hidden_in.astype(jnp.float32).reshape(N_DP, TOK_DEV, D)
    upstream_all = out_grad.astype(jnp.float32).reshape(N_DP, TOK_DEV, D) * target

    def group_step(totals, operands):
        rows_in, upstream, valid_group = operands
        valid_blocks = valid_group.reshape(block_count, per_block, SLOT)
        outputs, pullback = jax.vjp(partial(forward, valid_blocks=valid_blocks), weights, rows_in)
        param_grads, row_grads = pullback(upstream)
        totals = jax.tree.map(jnp.add, totals, param_grads)
        return (totals, (outputs.astype(jnp.bfloat16), row_grads.astype(jnp.bfloat16)))
    zero_grads = jax.tree.map(jnp.zeros_like, weights)
    totals, (outputs, row_grads) = lax.scan(group_step, zero_grads, (rows_all, upstream_all, valid_all))
    grad_qkv, grad_qvb, grad_outw, grad_outb, grad_gain1, grad_shift1, grad_upw, grad_upb, grad_downw, grad_downb, grad_gain2, grad_shift2 = totals
    return (outputs.reshape(TOKENS, D), row_grads.reshape(TOKENS, D), grad_qkv, grad_qvb, grad_outw, grad_outb, grad_gain1, grad_shift1, grad_upw, grad_upb, grad_downw, grad_downb, grad_gain2, grad_shift2)
```

```python
import jax
import jax.numpy as jnp
from jax import lax
from jax.sharding import PartitionSpec as P

HD = 64


EPSILON = 1e-05
ROOT_HALF = 0.7071067811865476
DENSITY = 0.3989422804014327
F32 = jnp.float32
BF16 = jnp.bfloat16


def norm_forward(hidden, norm_gain, norm_offset):
    average = jnp.mean(hidden, axis=1, keepdims=True)
    centred = hidden - average
    spread = jnp.mean(centred * centred, axis=1, keepdims=True)
    inverse = lax.rsqrt(spread + EPSILON)
    normal = centred * inverse
    return (normal * norm_gain + norm_offset, normal, inverse)


def norm_backward(upstream, normal, inverse, norm_gain):
    scaled = upstream * norm_gain
    first_mean = jnp.mean(scaled, axis=1, keepdims=True)
    second_mean = jnp.mean(scaled * normal, axis=1, keepdims=True)
    return inverse * (scaled - first_mean - normal * second_mean)


def gelu_parts(before):
    cumulative = 0.5 * (1.0 + jax.scipy.special.erf(before * ROOT_HALF))
    density = DENSITY * jnp.exp(-0.5 * before * before)
    return (before * cumulative, cumulative + before * density)


def body(
    hidden_in,
    qkv_weight,
    qv_bias,
    out_weight,
    out_bias,
    norm1_gain,
    norm1_shift,
    up_weight,
    up_bias,
    down_weight,
    down_bias,
    norm2_gain,
    norm2_shift,
    out_grad,
    seq_lengths,
    key_mask,
    split_pos,
):
    rows = hidden_in.shape[0]
    part_count = lax.axis_size("tensor")
    part_index = lax.axis_index("tensor")
    group_slots = seq_lengths.shape[0]
    slot_len = rows * part_count // group_slots
    slots = rows // slot_len
    width = hidden_in.shape[1]
    heads = width // HD

    w_qkv = lax.all_gather(qkv_weight, "tensor", axis=1, tiled=True)
    b_qv = lax.all_gather(qv_bias, "tensor", axis=1, tiled=True)
    w_out = lax.all_gather(out_weight, "tensor", axis=0, tiled=True)
    w_up = lax.all_gather(up_weight, "tensor", axis=0, tiled=True)
    b_up = lax.all_gather(up_bias, "tensor", axis=0, tiled=True)
    w_down = lax.all_gather(down_weight, "tensor", axis=0, tiled=True)

    lengths = lax.dynamic_slice_in_dim(seq_lengths, part_index * slots, slots)
    splits = lax.dynamic_slice_in_dim(split_pos, part_index * slots, slots)
    mask = lax.dynamic_slice_in_dim(key_mask, part_index * rows, rows).reshape(slots, slot_len)
    places = lax.broadcasted_iota(jnp.int32, (slots, slot_len), 1)
    valid = (places < lengths[:, None]) & ((mask == 1) | (places == 0))
    target = (
        ((places >= splits[:, None]) & (places < lengths[:, None])).astype(F32).reshape(rows, 1)
    )
    gain_mid = norm1_gain.astype(F32)
    shift_mid = norm1_shift.astype(F32)
    gain_out = norm2_gain.astype(F32)
    shift_out = norm2_shift.astype(F32)

    projected = jnp.einsum("rd,cld->crl", hidden_in, w_qkv, preferred_element_type=F32)
    bias_rows = jnp.stack([b_qv[0], jnp.zeros_like(b_qv[0]), b_qv[1]]).astype(F32)
    projected = (projected + bias_rows[:, None, :]).astype(BF16)
    head_shape = (slots, slot_len, heads, HD)
    queries = projected[0].reshape(head_shape)
    key_rows = projected[1].reshape(head_shape)
    value_rows = projected[2].reshape(head_shape)
    scores = jnp.einsum("sqhe,skhe->shqk", queries, key_rows, preferred_element_type=F32) * (
        HD ** (-0.5)
    )
    masked = jnp.where(valid[:, None, None, :], scores, -1e30)
    largest = jnp.max(masked, axis=-1, keepdims=True)
    weights_raw = jnp.exp(masked - largest)
    totals = jnp.sum(weights_raw, axis=-1, keepdims=True)
    probability = weights_raw / totals
    prob_low = probability.astype(BF16)
    context = jnp.einsum("shqk,skhe->sqhe", prob_low, value_rows, preferred_element_type=F32)
    context_rows = context.astype(BF16).reshape(rows, width)
    attn_out = jnp.dot(context_rows, w_out, preferred_element_type=F32)
    first_sum = hidden_in.astype(F32) + attn_out + out_bias.astype(F32)
    mid_rows, mid_normal, mid_inverse = norm_forward(first_sum, gain_mid, shift_mid)
    mid_low = mid_rows.astype(BF16)
    before = jnp.einsum("rd,fd->rf", mid_low, w_up, preferred_element_type=F32) + b_up.astype(F32)
    activated, gelu_slope = gelu_parts(before)
    activated_low = activated.astype(BF16)
    ffn_out = jnp.dot(activated_low, w_down, preferred_element_type=F32)
    second_sum = mid_rows + ffn_out + down_bias.astype(F32)
    out_rows, out_normal, out_inverse = norm_forward(second_sum, gain_out, shift_out)
    layer_out = out_rows.astype(BF16)

    upstream = out_grad.astype(F32) * target
    grad_gain_out = jnp.sum(upstream * out_normal, axis=0)
    grad_shift_out = jnp.sum(upstream, axis=0)
    second_grad = norm_backward(upstream, out_normal, out_inverse, gain_out)
    grad_down_bias = jnp.sum(second_grad, axis=0)
    second_low = second_grad.astype(BF16)
    grad_down = jnp.einsum("rf,rd->fd", activated_low, second_low, preferred_element_type=F32)
    grad_down = lax.psum(lax.psum_scatter(grad_down, "tensor", scatter_dimension=0, tiled=True), "dp")
    activated_grad = jnp.einsum("rd,fd->rf", second_low, w_down, preferred_element_type=F32)
    before_low = (activated_grad * gelu_slope).astype(BF16)
    grad_up = jnp.einsum("rf,rd->fd", before_low, mid_low, preferred_element_type=F32)
    grad_up_bias = jnp.sum(before_low, axis=0, dtype=F32)
    grad_up = lax.psum(lax.psum_scatter(grad_up, "tensor", scatter_dimension=0, tiled=True), "dp")
    grad_up_bias = lax.psum(
        lax.psum_scatter(grad_up_bias, "tensor", scatter_dimension=0, tiled=True), "dp"
    )
    mid_grad = second_grad + jnp.dot(before_low, w_up, preferred_element_type=F32)
    grad_gain_mid = jnp.sum(mid_grad * mid_normal, axis=0)
    grad_shift_mid = jnp.sum(mid_grad, axis=0)
    first_grad = norm_backward(mid_grad, mid_normal, mid_inverse, gain_mid)
    grad_out_bias = jnp.sum(first_grad, axis=0)
    first_low = first_grad.astype(BF16)
    grad_out_weight = jnp.einsum("rl,rd->ld", context_rows, first_low, preferred_element_type=F32)
    grad_out_weight = lax.psum(
        lax.psum_scatter(grad_out_weight, "tensor", scatter_dimension=0, tiled=True), "dp"
    )
    context_grad = (
        jnp.einsum("rd,ld->rl", first_low, w_out, preferred_element_type=F32)
        .astype(BF16)
        .reshape(head_shape)
    )
    prob_grad = jnp.einsum(
        "sqhe,skhe->shqk", context_grad, value_rows, preferred_element_type=F32
    )
    inner_sum = jnp.sum(probability * prob_grad, axis=-1, keepdims=True)
    score_grad = (probability * (prob_grad - inner_sum)).astype(BF16)
    query_grad = jnp.einsum(
        "shqk,skhe->sqhe", score_grad, key_rows, preferred_element_type=F32
    ) * (HD ** (-0.5))
    key_grad = jnp.einsum(
        "shqk,sqhe->skhe", score_grad, queries, preferred_element_type=F32
    ) * (HD ** (-0.5))
    value_grad = jnp.einsum("shqk,sqhe->skhe", prob_low, context_grad, preferred_element_type=F32)
    projected_grad = jnp.stack(
        [
            query_grad.reshape(rows, width),
            key_grad.reshape(rows, width),
            value_grad.reshape(rows, width),
        ]
    ).astype(BF16)
    grad_qkv = jnp.einsum("crl,rd->cld", projected_grad, hidden_in, preferred_element_type=F32)
    bias_sums = jnp.sum(projected_grad, axis=1, dtype=F32)
    grad_qv_bias = jnp.stack([bias_sums[0], bias_sums[2]])
    input_grad = (
        first_grad
        + jnp.einsum("crl,cld->rd", projected_grad, w_qkv, preferred_element_type=F32)
    ).astype(BF16)
    grad_qkv = lax.psum(lax.psum_scatter(grad_qkv, "tensor", scatter_dimension=1, tiled=True), "dp")
    grad_qv_bias = lax.psum(
        lax.psum_scatter(grad_qv_bias, "tensor", scatter_dimension=1, tiled=True), "dp"
    )
    grad_out_bias, grad_gain_mid, grad_shift_mid, grad_down_bias, grad_gain_out, grad_shift_out = (
        lax.psum(
            (
                grad_out_bias,
                grad_gain_mid,
                grad_shift_mid,
                grad_down_bias,
                grad_gain_out,
                grad_shift_out,
            ),
            ("dp", "tensor"),
        )
    )
    return (
        layer_out,
        input_grad,
        grad_qkv,
        grad_qv_bias,
        grad_out_weight,
        grad_out_bias,
        grad_gain_mid,
        grad_shift_mid,
        grad_up,
        grad_up_bias,
        grad_down,
        grad_down_bias,
        grad_gain_out,
        grad_shift_out,
    )


def solution(mesh):
    in_specs = (
        P(("dp", "tensor"), None),
        P(None, "tensor", None),
        P(None, "tensor"),
        P("tensor", None),
        P(),
        P(),
        P(),
        P("tensor", None),
        P("tensor"),
        P("tensor", None),
        P(),
        P(),
        P(),
        P(("dp", "tensor"), None),
        P("dp"),
        P("dp"),
        P("dp"),
    )
    out_specs = (
        P(("dp", "tensor"), None),
        P(("dp", "tensor"), None),
        P(None, "tensor", None),
        P(None, "tensor"),
        P("tensor", None),
        P(),
        P(),
        P(),
        P("tensor", None),
        P("tensor"),
        P("tensor", None),
        P(),
        P(),
        P(),
    )
    return jax.shard_map(body, mesh=mesh, in_specs=in_specs, out_specs=out_specs, check_vma=False)
```
